128 devices in a mesh: outer: 8 (over z, core), inner: 16 (over x, y).
Axes of the slice: x: 4, y: 4, z: 4, core: 2. Of those that a mesh axis runs over, the one named last changes fastest.
Arguments:
- child_update: float32 [8, 2048, 2048], P('outer', 'inner'), may hold values from -1 to 8, as said below
- block_map: int32 [2, 8, 16], replicated, may hold values from 0 to 23, as said below
- obs_design: bfloat16 [262144, 128], P(('outer', 'inner')), may hold values from -2 to 2
- obs_target: int32 [262144], P(('outer', 'inner')), may hold values from 0 to 47
Outputs:
- pivot_factor: float32 [2, 8, 1024, 1024], P(None, 'outer', 'inner')
- border_factor: float32 [2, 8, 2048, 1024], P(None, 'outer', 'inner')
- top_update: float32 [8, 2048, 2048], P('outer', 'inner')
The draws below stay inside these ranges and needn't reach their ends.
Inputs may be any that keep to these rules, and one draw needn't show every extreme that they name: `child_update`: each group's matrix is symmetric and positive definite. `block_map`: entry [l, g] names distinct parent blocks for the blocks of one child; groups under the same child hold equal entries; the two children of a parent together name every parent block.
All inputs are finite; a program needn't handle non-finite values.
Results may differ from the reference program's by a relative error of at most 0.0003.
Values sent between devices are 32-bit elements; how exact they have to be, the bound alone decides.
No kernel may reach another device: no remote copies, remote signals or barrier semaphores. Data moves between devices by JAX's collectives and lax.ppermute only.
A program may use at most 128 MiB of HBM per device.

```python
import math
import jax
import jax.numpy as jnp
import numpy as np
from jax import lax

S = 1024
B = 2048
BLK = 128
LEVELS = 2
GROUPS = 8
OBS = 262144
TARGETS = 48


def draw_child_update(key, part):
    key_points, key_noise, key_diag = jax.random.split(key, 3)
    points = jax.random.uniform(key_points, (GROUPS, B, 3), jnp.float32)
    squared = jnp.zeros((GROUPS, B, B), jnp.float32)
    for axis_index in range(3):
        coords = points[:, :, axis_index]
        squared = squared + (coords[:, :, None] - coords[:, None, :]) ** 2
    length_scale = (0.64 / B) ** (1.0 / 3.0)
    kernel = jnp.exp(-jnp.sqrt(squared) / length_scale)
    identity = jnp.eye(B, dtype=jnp.float32)[None, :, :]
    raw_noise = jax.random.uniform(key_noise, (GROUPS, B, B), jnp.float32, -1.0, 1.0)
    diagonal = 2.0 + 2.0 * jax.random.uniform(key_diag, (GROUPS, B), jnp.float32)
    weight = 0.5
    noise = (raw_noise + jnp.swapaxes(raw_noise, 1, 2)) * (1.0 / B)
    matrix = weight * kernel + noise * (1.0 - identity) + identity * diagonal[:, :, None]
    return matrix.astype(jnp.float32)


def draw_block_map(key, part):
    parent_count = (S + B) // BLK
    child_count = B // BLK
    sep_count = S // BLK
    level_rows = []
    for level_index in range(LEVELS):
        level_key = jax.random.fold_in(key, level_index)

        def front_order(front_index):
            return jax.random.permutation(jax.random.fold_in(level_key, front_index), parent_count)
        orders = jax.vmap(front_order)(jnp.arange(GROUPS, dtype=jnp.int32))
        group_ids = jnp.arange(GROUPS, dtype=jnp.int32)
        front_ids = group_ids >> level_index + 1
        child_side = group_ids >> level_index & 1
        chosen = orders[front_ids]
        picked_slots = child_side[:, None] * sep_count + jnp.arange(child_count, dtype=jnp.int32)[None, :]
        level_rows.append(jnp.take_along_axis(chosen, picked_slots, axis=1))
    return jnp.stack(level_rows).astype(jnp.int32)


def draw_obs_design(key, part):
    key_values = jax.random.fold_in(key, 0)
    base_scale = (0.46 * TARGETS / OBS) ** 0.5
    position = jnp.arange(OBS, dtype=jnp.float32) / OBS
    rising = 1.0 + 2.0 * position
    values = jnp.clip(jax.random.normal(key_values, (OBS, BLK), jnp.float32), -4.0, 4.0)
    design = values * (base_scale * rising)[:, None]
    return design.astype(jnp.bfloat16)


def touch_ends(result, key, low, high):
    shape = result.shape
    index_at = [jax.random.randint(jax.random.fold_in(key, axis), (), 0, shape[axis]) for axis in range(len(shape))]
    result = result.at[tuple(index_at)].set(low)
    longest = shape.index(max(shape))
    index_at[longest] = (index_at[longest] + 1) % shape[longest]
    return result.at[tuple(index_at)].set(high)


def rank_bounds(count, lean):
    weights = [(1 << 20) // math.isqrt(grade ** lean) + 1 for grade in range(1, count + 1)]
    spread = 1 + sum(weights) // (1 << 30)
    return np.cumsum(np.array([max(1, weight // spread) for weight in weights]))


def skewed_ids(own_key, shape, number_of, lean):
    listing = rank_bounds(number_of, lean)
    pick = jax.random.randint(jax.random.fold_in(own_key, 1), shape, 0, int(listing[number_of - 1]))
    rank = jnp.searchsorted(jnp.asarray(listing, jnp.int32), pick, side="right")
    return jax.random.permutation(jax.random.fold_in(own_key, 2), number_of)[rank].astype(jnp.int32)


def setup_inputs(seed: int = 0) -> dict:
    seeds = jax.random.split(jax.random.key(seed), 5)
    child_update = draw_child_update(jax.random.fold_in(seeds[4], 71), 0)
    block_map = draw_block_map(jax.random.fold_in(seeds[4], 71), 0)
    obs_design = draw_obs_design(jax.random.fold_in(seeds[4], 71), 0)
    obs_target = touch_ends(skewed_ids(seeds[3], (OBS,), TARGETS, 2), jax.random.fold_in(seeds[3], 3), 0, TARGETS - 1).astype(jnp.int32)
    return {"child_update": child_update, "block_map": block_map, "obs_design": obs_design, "obs_target": obs_target}


HIGHEST = lax.Precision.HIGHEST

def observation_blocks(obs_design, obs_target):

    def one_target(target_index):
        chosen = jnp.where((obs_target == target_index)[:, None], obs_design, jnp.zeros_like(obs_design))
        return jnp.dot(chosen.T.astype(jnp.float32), obs_design.astype(jnp.float32), preferred_element_type=jnp.float32)
    return lax.map(one_target, jnp.arange(TARGETS, dtype=jnp.int32))

def place_child(front_matrix, update, child_map):
    flat_index = (child_map[:, None] * BLK + jnp.arange(BLK, dtype=jnp.int32)[None, :]).reshape(-1)
    return front_matrix.at[flat_index[:, None], flat_index[None, :]].add(update)

def reference(child_update, block_map, obs_design, obs_target):
    gram_blocks = observation_blocks(obs_design, obs_target)
    sep_blocks = S // BLK
    updates = child_update
    pivot_levels = []
    border_levels = []
    front_base = 0
    for level_index in range(LEVELS):
        front_count = GROUPS >> level_index + 1
        level_pivots = []
        level_borders = []
        level_updates = []
        for front_index in range(front_count):
            front_matrix = jnp.zeros((S + B, S + B), jnp.float32)
            for child_side in range(2):
                child_index = 2 * front_index + child_side
                child_map = block_map[level_index, child_index << level_index]
                front_matrix = place_child(front_matrix, updates[child_index], child_map)
            for block_index in range(sep_blocks):
                first_row = block_index * BLK
                gram_one = gram_blocks[(front_base + front_index) * sep_blocks + block_index]
                front_matrix = front_matrix.at[first_row:first_row + BLK, first_row:first_row + BLK].add(gram_one)
            pivot_lower = jnp.linalg.cholesky(front_matrix[:S, :S])
            border_rows = jax.scipy.linalg.solve_triangular(pivot_lower, front_matrix[S:, :S].T, lower=True).T
            complement = front_matrix[S:, S:] - jnp.dot(border_rows.astype(jnp.float32), border_rows.T.astype(jnp.float32), precision=HIGHEST, preferred_element_type=jnp.float32)
            level_pivots.append(pivot_lower)
            level_borders.append(border_rows)
            level_updates.append(complement)
        front_base = front_base + front_count
        updates = jnp.stack(level_updates)
        repeat_count = 2 ** (level_index + 1)
        pivot_levels.append(jnp.repeat(jnp.stack(level_pivots), repeat_count, axis=0))
        border_levels.append(jnp.repeat(jnp.stack(level_borders), repeat_count, axis=0))
    top_update = jnp.repeat(updates, 2 ** LEVELS, axis=0)
    return (jnp.stack(pivot_levels), jnp.stack(border_levels), top_update)
```

```python
import math

import jax
import jax.numpy as jnp
from jax import lax
from jax.sharding import PartitionSpec as P

S = 1024
B = 2048
BLK = 128
LEVELS = 2


HIGHEST = lax.Precision.HIGHEST


def partner_2(block, axis, bit):
    count = lax.axis_size(axis)
    route = []
    for low in range(count):
        high = low | 1 << bit
        if high != low and high < count:
            route += [(low, high), (high, low)]
    return lax.ppermute(block, axis, route)


def block_source(child_map, parent_count):
    child_count = child_map.shape[0]
    matches = child_map[:, None] == jnp.arange(parent_count, dtype=jnp.int32)[None, :]
    source = jnp.sum(
        jnp.where(matches, jnp.arange(child_count, dtype=jnp.int32)[:, None], 0), axis=0
    )
    present = jnp.any(matches, axis=0)
    return (source, present)


def parent_columns(child_rows, child_map, parent_count):
    row_count = child_rows.shape[0]
    child_count = child_map.shape[0]
    block_size = child_rows.shape[1] // child_count
    source, present = block_source(child_map, parent_count)
    blocks = child_rows.reshape(row_count, child_count, block_size)
    picked = jnp.take(blocks, source, axis=1)
    picked = jnp.where(present[None, :, None], picked, jnp.zeros_like(picked))
    return picked.reshape(row_count, parent_count * block_size)


def parent_rows(child_cols, child_map, parent_count):
    col_count = child_cols.shape[1]
    child_count = child_map.shape[0]
    block_size = child_cols.shape[0] // child_count
    source, present = block_source(child_map, parent_count)
    blocks = child_cols.reshape(child_count, block_size, col_count)
    picked = jnp.take(blocks, source, axis=0)
    picked = jnp.where(present[:, None, None], picked, jnp.zeros_like(picked))
    return picked.reshape(parent_count * block_size, col_count)


def owner_major(parent_cols, inner_count):
    row_count = parent_cols.shape[0]
    sep_part = parent_cols[:, :S].reshape(row_count, inner_count, S // inner_count)
    border_part = parent_cols[:, S:].reshape(row_count, inner_count, B // inner_count)
    return jnp.concatenate([sep_part, border_part], axis=2)


def blocked_cholesky(matrix, panel_size):
    order = matrix.shape[0]
    lower_factor = jnp.zeros_like(matrix)
    trailing = matrix
    inverse_list = []
    for panel_index in range(order // panel_size):
        first = panel_index * panel_size
        last = first + panel_size
        diagonal_block = trailing[first:last, first:last]
        panel_lower = jnp.linalg.cholesky(diagonal_block)
        identity = jnp.eye(panel_size, dtype=jnp.float32)
        inverse = jax.scipy.linalg.solve_triangular(panel_lower, identity, lower=True)
        inverse_list.append(inverse)
        lower_factor = lower_factor.at[first:last, first:last].set(panel_lower)
        if last < order:
            below = jnp.dot(
                trailing[last:, first:last],
                inverse.T,
                precision=HIGHEST,
                preferred_element_type=jnp.float32,
            )
            lower_factor = lower_factor.at[last:, first:last].set(below)
            update = jnp.dot(below, below.T, precision=HIGHEST, preferred_element_type=jnp.float32)
            trailing = trailing.at[last:, last:].add(-update)
    return (lower_factor, inverse_list)


def cholesky_inverse(matrix, base_size):
    order = matrix.shape[0]
    if order <= base_size:
        lower = jnp.linalg.cholesky(matrix)
        identity = jnp.eye(order, dtype=jnp.float32)
        return (lower, jax.scipy.linalg.solve_triangular(lower, identity, lower=True))
    half = order // 2
    lower_11, inverse_11 = cholesky_inverse(matrix[:half, :half], base_size)
    lower_21 = jnp.dot(matrix[half:, :half], inverse_11.T, precision=HIGHEST, preferred_element_type=jnp.float32)
    schur = matrix[half:, half:] - jnp.dot(lower_21, lower_21.T, precision=HIGHEST, preferred_element_type=jnp.float32)
    lower_22, inverse_22 = cholesky_inverse(schur, base_size)
    inverse_21 = -jnp.dot(
        inverse_22,
        jnp.dot(lower_21, inverse_11, precision=HIGHEST, preferred_element_type=jnp.float32),
        precision=HIGHEST,
        preferred_element_type=jnp.float32,
    )
    zero = jnp.zeros((half, half), jnp.float32)
    lower = jnp.block([[lower_11, zero], [lower_21, lower_22]])
    inverse = jnp.block([[inverse_11, zero], [inverse_21, inverse_22]])
    return (lower, inverse)


def border_solve(rows_in, lower_factor, inverse_list, panel_size):
    solved = []
    for panel_index in range(len(inverse_list)):
        first = panel_index * panel_size
        pending = rows_in[:, first : first + panel_size]
        for earlier in range(panel_index):
            coupling = lower_factor[
                first : first + panel_size, earlier * panel_size : (earlier + 1) * panel_size
            ]
            pending = pending - jnp.dot(
                solved[earlier], coupling.T, precision=HIGHEST, preferred_element_type=jnp.float32
            )
        solved.append(
            jnp.dot(
                pending,
                inverse_list[panel_index].T,
                precision=HIGHEST,
                preferred_element_type=jnp.float32,
            )
        )
    return jnp.concatenate(solved, axis=1)


def shards(child_update, block_map, obs_design, obs_target):
    inner_count = lax.axis_size("inner")
    group_count = lax.axis_size("outer")
    group_index = lax.axis_index("outer")
    member = lax.axis_index("inner")
    parent_count = (S + B) // BLK
    sep_rows = S // inner_count
    sep_blocks = S // BLK
    panel_size = min(S, 256)
    front_total = sum((group_count >> level_index + 1 for level_index in range(LEVELS)))
    target_total = front_total * sep_blocks
    row_count = obs_design.shape[0]
    step_rows = math.gcd(row_count, 256)
    target_ids = jnp.arange(target_total, dtype=jnp.int32)

    def add_rows(block_index, running):
        design = lax.dynamic_slice_in_dim(obs_design, block_index * step_rows, step_rows, 0)
        labels = lax.dynamic_slice_in_dim(obs_target, block_index * step_rows, step_rows, 0)
        selector = (labels[:, None] == target_ids[None, :]).astype(jnp.bfloat16)
        spread = selector[:, :, None] * design[:, None, :]
        return running + jnp.einsum(
            "rtj,rk->tjk", spread, design, preferred_element_type=jnp.float32
        )

    gram_blocks = lax.fori_loop(
        0, row_count // step_rows, add_rows, jnp.zeros((target_total, BLK, BLK), jnp.float32)
    )
    per_front = gram_blocks.reshape(front_total, S, BLK)
    obs_share = lax.psum(lax.psum_scatter(per_front, "inner", scatter_dimension=1, tiled=True), "outer")
    current = child_update[0]
    pivot_list = []
    border_list = []
    front_offset = 0
    block_start = member * sep_rows // BLK * BLK
    for level_index in range(LEVELS):
        partner = group_index ^ 1 << level_index
        level_maps = block_map[level_index]
        own_map = lax.dynamic_index_in_dim(level_maps, group_index, 0, keepdims=False)
        sib_map = lax.dynamic_index_in_dim(level_maps, partner, 0, keepdims=False)
        sibling = partner_2(current, "outer", level_index)
        outgoing = jnp.stack(
            [
                owner_major(parent_columns(current, own_map, parent_count), inner_count),
                owner_major(parent_columns(sibling, sib_map, parent_count), inner_count),
            ]
        )
        arrived = lax.all_to_all(outgoing, "inner", split_axis=2, concat_axis=1, tiled=True)
        own_cols = parent_rows(arrived[0, :, 0, :], own_map, parent_count)
        sib_cols = parent_rows(arrived[1, :, 0, :], sib_map, parent_count)
        front_rows = (own_cols + sib_cols).T
        front_slot = front_offset + (group_index >> level_index + 1)
        obs_rows = lax.dynamic_index_in_dim(obs_share, front_slot, 0, keepdims=False)
        sep_front = front_rows[:sep_rows]
        block_now = lax.dynamic_slice_in_dim(sep_front, block_start, BLK, 1)
        sep_front = lax.dynamic_update_slice_in_dim(sep_front, block_now + obs_rows, block_start, 1)
        front_offset = front_offset + (group_count >> level_index + 1)
        pivot_all = lax.all_gather(sep_front[:, :S], "inner", axis=0, tiled=True)
        border_front = front_rows[sep_rows:]
        coupling_all = lax.all_gather(border_front[:, :S], "inner", axis=0, tiled=True)
        pivot_lower, pivot_inverse = cholesky_inverse(pivot_all, BLK)
        border_all = jnp.dot(
            coupling_all, pivot_inverse.T, precision=HIGHEST, preferred_element_type=jnp.float32
        )
        border_factor = lax.dynamic_slice_in_dim(border_all, member * (B // inner_count), B // inner_count, 0)
        product = jnp.einsum(
            "rs,cs->rc",
            border_factor,
            border_all,
            precision=HIGHEST,
            preferred_element_type=jnp.float32,
        )
        current = border_front[:, S:] - product
        pivot_list.append(lax.dynamic_slice_in_dim(pivot_lower, member * sep_rows, sep_rows, 0))
        border_list.append(border_factor)
    pivot_factor = jnp.stack(pivot_list)[:, None]
    border_out = jnp.stack(border_list)[:, None]
    return (pivot_factor, border_out, current[None])


def solution(mesh):
    in_specs = (P("outer", "inner", None), P(), P(("outer", "inner"), None), P(("outer", "inner")))
    out_specs = (
        P(None, "outer", "inner", None),
        P(None, "outer", "inner", None),
        P("outer", "inner", None),
    )
    return jax.shard_map(shards, mesh=mesh, in_specs=in_specs, out_specs=out_specs, check_vma=False)
```

```python
import math

import jax
import jax.numpy as jnp
from jax import lax
from jax.experimental import pallas as pl
from jax.experimental.pallas import tpu as pltpu
from jax.sharding import PartitionSpec as P

S = 1024
B = 2048
BLK = 128
LEVELS = 2


HIGHEST = lax.Precision.HIGHEST
HIGH = lax.Precision.HIGH
SUB = 8

def _outer_t(left, right):
    return lax.dot_general(left, right, (((0,), (0,)), ((), ())), precision=HIGHEST, preferred_element_type=jnp.float32)

def _kernel(a_ref, l_ref, x_ref, w_ref, t_ref):
    n = a_ref.shape[0]
    row = lax.broadcasted_iota(jnp.int32, (n, n), 0)
    col = lax.broadcasted_iota(jnp.int32, (n, n), 1)
    a = a_ref[...]
    w_ref[...] = jnp.where(row >= col, a, a.T)
    x_ref[...] = jnp.where(row == col, 1.0, 0.0).astype(jnp.float32)
    sub = lax.broadcasted_iota(jnp.int32, (SUB, n), 0)
    lane = lax.broadcasted_iota(jnp.int32, (SUB, n), 1)
    lane1 = lax.broadcasted_iota(jnp.int32, (1, n), 1)
    sub1 = lax.broadcasted_iota(jnp.int32, (SUB, 1), 0)

    for jb in range(n // SUB):
        r0 = jb * SUB
        rows = w_ref[pl.ds(r0, SUB), :]
        xb = x_ref[pl.ds(r0, SUB), :]
        panel = jnp.zeros((SUB, n), jnp.float32)
        for i in range(SUB):
            c = r0 + i
            ri = rows[i : i + 1, :]
            piv = ri[:, c : c + 1]
            s = lax.rsqrt(piv)
            li = jnp.where(lane1 >= c, ri * s, 0.0)
            rc = rows[:, c : c + 1]
            lk = jnp.where(sub1 > i, rc * s, 0.0)
            rows = rows - lk * li
            panel = jnp.where(sub == i, li, panel)
            xi = xb[i : i + 1, :] * s
            xb = jnp.where(sub == i, xi, xb - lk * xi)
        t_ref[pl.ds(r0, SUB), :] = panel
        x_ref[pl.ds(r0, SUB), :] = xb
        w_ref[...] = w_ref[...] - _outer_t(panel, panel)
        below = row >= r0 + SUB
        x_now = x_ref[...]
        x_ref[...] = jnp.where(below, x_now - _outer_t(panel, xb), x_now)
    l_ref[...] = t_ref[...].T

def base_cholesky_inverse(a):
    n = a.shape[0]
    return pl.pallas_call(
        _kernel,
        out_shape=(jax.ShapeDtypeStruct((n, n), jnp.float32), jax.ShapeDtypeStruct((n, n), jnp.float32)),
        scratch_shapes=[pltpu.VMEM((n, n), jnp.float32), pltpu.VMEM((n, n), jnp.float32)],
    )(a)


def partner_2(block, axis, bit):
    count = lax.axis_size(axis)
    route = []
    for low in range(count):
        high = low | 1 << bit
        if high != low and high < count:
            route += [(low, high), (high, low)]
    return lax.ppermute(block, axis, route)


def block_source(child_map, parent_count):
    child_count = child_map.shape[0]
    matches = child_map[:, None] == jnp.arange(parent_count, dtype=jnp.int32)[None, :]
    source = jnp.sum(
        jnp.where(matches, jnp.arange(child_count, dtype=jnp.int32)[:, None], 0), axis=0
    )
    present = jnp.any(matches, axis=0)
    return (source, present)


def parent_columns(child_rows, child_map, parent_count):
    row_count = child_rows.shape[0]
    child_count = child_map.shape[0]
    block_size = child_rows.shape[1] // child_count
    source, present = block_source(child_map, parent_count)
    blocks = child_rows.reshape(row_count, child_count, block_size)
    picked = jnp.take(blocks, source, axis=1)
    picked = jnp.where(present[None, :, None], picked, jnp.zeros_like(picked))
    return picked.reshape(row_count, parent_count * block_size)


def parent_rows(child_cols, child_map, parent_count):
    col_count = child_cols.shape[1]
    child_count = child_map.shape[0]
    block_size = child_cols.shape[0] // child_count
    source, present = block_source(child_map, parent_count)
    blocks = child_cols.reshape(child_count, block_size, col_count)
    picked = jnp.take(blocks, source, axis=0)
    picked = jnp.where(present[:, None, None], picked, jnp.zeros_like(picked))
    return picked.reshape(parent_count * block_size, col_count)


def owner_major(parent_cols, inner_count):
    row_count = parent_cols.shape[0]
    sep_part = parent_cols[:, :S].reshape(row_count, inner_count, S // inner_count)
    border_part = parent_cols[:, S:].reshape(row_count, inner_count, B // inner_count)
    return jnp.concatenate([sep_part, border_part], axis=2)


def blocked_cholesky(matrix, panel_size):
    order = matrix.shape[0]
    lower_factor = jnp.zeros_like(matrix)
    trailing = matrix
    inverse_list = []
    for panel_index in range(order // panel_size):
        first = panel_index * panel_size
        last = first + panel_size
        diagonal_block = trailing[first:last, first:last]
        panel_lower = jnp.linalg.cholesky(diagonal_block)
        identity = jnp.eye(panel_size, dtype=jnp.float32)
        inverse = jax.scipy.linalg.solve_triangular(panel_lower, identity, lower=True)
        inverse_list.append(inverse)
        lower_factor = lower_factor.at[first:last, first:last].set(panel_lower)
        if last < order:
            below = jnp.dot(
                trailing[last:, first:last],
                inverse.T,
                precision=HIGHEST,
                preferred_element_type=jnp.float32,
            )
            lower_factor = lower_factor.at[last:, first:last].set(below)
            update = jnp.dot(below, below.T, precision=HIGHEST, preferred_element_type=jnp.float32)
            trailing = trailing.at[last:, last:].add(-update)
    return (lower_factor, inverse_list)


def cholesky_inverse(matrix, base_size):
    order = matrix.shape[0]
    if order <= base_size:
        return base_cholesky_inverse(matrix)
    half = order // 2
    lower_11, inverse_11 = cholesky_inverse(matrix[:half, :half], base_size)
    lower_21 = jnp.dot(matrix[half:, :half], inverse_11.T, precision=HIGHEST, preferred_element_type=jnp.float32)
    schur = matrix[half:, half:] - jnp.dot(lower_21, lower_21.T, precision=HIGHEST, preferred_element_type=jnp.float32)
    lower_22, inverse_22 = cholesky_inverse(schur, base_size)
    inverse_21 = -jnp.dot(
        inverse_22,
        jnp.dot(lower_21, inverse_11, precision=HIGHEST, preferred_element_type=jnp.float32),
        precision=HIGHEST,
        preferred_element_type=jnp.float32,
    )
    zero = jnp.zeros((half, half), jnp.float32)
    lower = jnp.block([[lower_11, zero], [lower_21, lower_22]])
    inverse = jnp.block([[inverse_11, zero], [inverse_21, inverse_22]])
    return (lower, inverse)


def border_solve(rows_in, lower_factor, inverse_list, panel_size):
    solved = []
    for panel_index in range(len(inverse_list)):
        first = panel_index * panel_size
        pending = rows_in[:, first : first + panel_size]
        for earlier in range(panel_index):
            coupling = lower_factor[
                first : first + panel_size, earlier * panel_size : (earlier + 1) * panel_size
            ]
            pending = pending - jnp.dot(
                solved[earlier], coupling.T, precision=HIGHEST, preferred_element_type=jnp.float32
            )
        solved.append(
            jnp.dot(
                pending,
                inverse_list[panel_index].T,
                precision=HIGHEST,
                preferred_element_type=jnp.float32,
            )
        )
    return jnp.concatenate(solved, axis=1)


def shards(child_update, block_map, obs_design, obs_target):
    inner_count = lax.axis_size("inner")
    group_count = lax.axis_size("outer")
    group_index = lax.axis_index("outer")
    member = lax.axis_index("inner")
    parent_count = (S + B) // BLK
    sep_rows = S // inner_count
    sep_blocks = S // BLK
    panel_size = min(S, 256)
    front_total = sum((group_count >> level_index + 1 for level_index in range(LEVELS)))
    target_total = front_total * sep_blocks
    row_count = obs_design.shape[0]
    step_rows = math.gcd(row_count, 256)
    target_ids = jnp.arange(target_total, dtype=jnp.int32)

    def add_rows(block_index, running):
        design = lax.dynamic_slice_in_dim(obs_design, block_index * step_rows, step_rows, 0)
        labels = lax.dynamic_slice_in_dim(obs_target, block_index * step_rows, step_rows, 0)
        selector = (labels[:, None] == target_ids[None, :]).astype(jnp.bfloat16)
        spread = selector[:, :, None] * design[:, None, :]
        return running + jnp.einsum(
            "rtj,rk->tjk", spread, design, preferred_element_type=jnp.float32
        )

    gram_blocks = lax.fori_loop(
        0, row_count // step_rows, add_rows, jnp.zeros((target_total, BLK, BLK), jnp.float32)
    )
    per_front = gram_blocks.reshape(front_total, S, BLK)
    obs_share = lax.psum_scatter(per_front, "inner", scatter_dimension=1, tiled=True)
    for bit in range(group_count.bit_length() - 1):
        obs_share = obs_share + partner_2(obs_share, "outer", bit)
    current = child_update[0]
    pivot_list = []
    border_list = []
    front_offset = 0
    block_start = member * sep_rows // BLK * BLK
    for level_index in range(LEVELS):
        partner = group_index ^ 1 << level_index
        level_maps = block_map[level_index]
        own_map = lax.dynamic_index_in_dim(level_maps, group_index, 0, keepdims=False)
        sib_map = lax.dynamic_index_in_dim(level_maps, partner, 0, keepdims=False)
        sibling = partner_2(current, "outer", level_index)
        outgoing = jnp.stack(
            [
                owner_major(parent_columns(current, own_map, parent_count), inner_count),
                owner_major(parent_columns(sibling, sib_map, parent_count), inner_count),
            ]
        )
        arrived = lax.all_to_all(outgoing, "inner", split_axis=2, concat_axis=1, tiled=True)
        own_cols = parent_rows(arrived[0, :, 0, :], own_map, parent_count)
        sib_cols = parent_rows(arrived[1, :, 0, :], sib_map, parent_count)
        front_rows = (own_cols + sib_cols).T
        front_slot = front_offset + (group_index >> level_index + 1)
        obs_rows = lax.dynamic_index_in_dim(obs_share, front_slot, 0, keepdims=False)
        sep_front = front_rows[:sep_rows]
        block_now = lax.dynamic_slice_in_dim(sep_front, block_start, BLK, 1)
        sep_front = lax.dynamic_update_slice_in_dim(sep_front, block_now + obs_rows, block_start, 1)
        front_offset = front_offset + (group_count >> level_index + 1)
        pivot_all = lax.all_gather(sep_front[:, :S], "inner", axis=0, tiled=True)
        border_front = front_rows[sep_rows:]
        coupling_all = lax.all_gather(border_front[:, :S], "inner", axis=0, tiled=True)
        pivot_lower, pivot_inverse = cholesky_inverse(pivot_all, BLK)
        border_all = jnp.dot(
            coupling_all, pivot_inverse.T, precision=HIGH, preferred_element_type=jnp.float32
        )
        border_factor = lax.dynamic_slice_in_dim(border_all, member * (B // inner_count), B // inner_count, 0)
        product = jnp.einsum(
            "rs,cs->rc",
            border_factor,
            border_all,
            precision=HIGH,
            preferred_element_type=jnp.float32,
        )
        current = border_front[:, S:] - product
        pivot_list.append(lax.dynamic_slice_in_dim(pivot_lower, member * sep_rows, sep_rows, 0))
        border_list.append(border_factor)
    pivot_factor = jnp.stack(pivot_list)[:, None]
    border_out = jnp.stack(border_list)[:, None]
    return (pivot_factor, border_out, current[None])


def solution(mesh):
    in_specs = (P("outer", "inner", None), P(), P(("outer", "inner"), None), P(("outer", "inner")))
    out_specs = (
        P(None, "outer", "inner", None),
        P(None, "outer", "inner", None),
        P("outer", "inner", None),
    )
    return jax.shard_map(shards, mesh=mesh, in_specs=in_specs, out_specs=out_specs, check_vma=False)
```

```python
import math

import jax
import jax.numpy as jnp
from jax import lax
from jax.experimental import pallas as pl
from jax.experimental.pallas import tpu as pltpu
from jax.sharding import PartitionSpec as P

S = 1024
B = 2048
BLK = 128
LEVELS = 2


HIGHEST = lax.Precision.HIGHEST
HIGH = lax.Precision.HIGH
SUB = 8

def _outer_t(left, right):
    return lax.dot_general(left, right, (((0,), (0,)), ((), ())), precision=HIGHEST, preferred_element_type=jnp.float32)

def _kernel(a_ref, l_ref, x_ref, w_ref, t_ref):
    n = a_ref.shape[0]
    row = lax.broadcasted_iota(jnp.int32, (n, n), 0)
    col = lax.broadcasted_iota(jnp.int32, (n, n), 1)
    a = a_ref[...]
    w_ref[...] = jnp.where(row >= col, a, a.T)
    x_ref[...] = jnp.where(row == col, 1.0, 0.0).astype(jnp.float32)
    sub = lax.broadcasted_iota(jnp.int32, (SUB, n), 0)
    lane = lax.broadcasted_iota(jnp.int32, (SUB, n), 1)
    lane1 = lax.broadcasted_iota(jnp.int32, (1, n), 1)
    sub1 = lax.broadcasted_iota(jnp.int32, (SUB, 1), 0)

    for jb in range(n // SUB):
        r0 = jb * SUB
        rows = w_ref[pl.ds(r0, SUB), :]
        xb = x_ref[pl.ds(r0, SUB), :]
        panel = jnp.zeros((SUB, n), jnp.float32)
        for i in range(SUB):
            c = r0 + i
            ri = rows[i : i + 1, :]
            piv = ri[:, c : c + 1]
            s = lax.rsqrt(piv)
            li = jnp.where(lane1 >= c, ri * s, 0.0)
            rc = rows[:, c : c + 1]
            lk = jnp.where(sub1 > i, rc * s, 0.0)
            rows = rows - lk * li
            panel = jnp.where(sub == i, li, panel)
            xi = xb[i : i + 1, :] * s
            xb = jnp.where(sub == i, xi, xb - lk * xi)
        t_ref[pl.ds(r0, SUB), :] = panel
        x_ref[pl.ds(r0, SUB), :] = xb
        w_ref[...] = w_ref[...] - _outer_t(panel, panel)
        below = row >= r0 + SUB
        x_now = x_ref[...]
        x_ref[...] = jnp.where(below, x_now - _outer_t(panel, xb), x_now)
    l_ref[...] = t_ref[...].T

def base_cholesky_inverse(a):
    n = a.shape[0]
    return pl.pallas_call(
        _kernel,
        out_shape=(jax.ShapeDtypeStruct((n, n), jnp.float32), jax.ShapeDtypeStruct((n, n), jnp.float32)),
        scratch_shapes=[pltpu.VMEM((n, n), jnp.float32), pltpu.VMEM((n, n), jnp.float32)],
    )(a)


def partner_2(block, axis, bit):
    count = lax.axis_size(axis)
    route = []
    for low in range(count):
        high = low | 1 << bit
        if high != low and high < count:
            route += [(low, high), (high, low)]
    return lax.ppermute(block, axis, route)


def block_source(child_map, parent_count):
    child_count = child_map.shape[0]
    matches = child_map[:, None] == jnp.arange(parent_count, dtype=jnp.int32)[None, :]
    source = jnp.sum(
        jnp.where(matches, jnp.arange(child_count, dtype=jnp.int32)[:, None], 0), axis=0
    )
    present = jnp.any(matches, axis=0)
    return (source, present)


def parent_columns(child_rows, child_map, parent_count):
    row_count = child_rows.shape[0]
    child_count = child_map.shape[0]
    block_size = child_rows.shape[1] // child_count
    source, present = block_source(child_map, parent_count)
    blocks = child_rows.reshape(row_count, child_count, block_size)
    picked = jnp.take(blocks, source, axis=1)
    picked = jnp.where(present[None, :, None], picked, jnp.zeros_like(picked))
    return picked.reshape(row_count, parent_count * block_size)


def parent_rows(child_cols, child_map, parent_count):
    col_count = child_cols.shape[1]
    child_count = child_map.shape[0]
    block_size = child_cols.shape[0] // child_count
    source, present = block_source(child_map, parent_count)
    blocks = child_cols.reshape(child_count, block_size, col_count)
    picked = jnp.take(blocks, source, axis=0)
    picked = jnp.where(present[:, None, None], picked, jnp.zeros_like(picked))
    return picked.reshape(parent_count * block_size, col_count)


def owner_major(parent_cols, inner_count):
    row_count = parent_cols.shape[0]
    sep_part = parent_cols[:, :S].reshape(row_count, inner_count, S // inner_count)
    border_part = parent_cols[:, S:].reshape(row_count, inner_count, B // inner_count)
    return jnp.concatenate([sep_part, border_part], axis=2)


def blocked_cholesky(matrix, panel_size):
    order = matrix.shape[0]
    lower_factor = jnp.zeros_like(matrix)
    trailing = matrix
    inverse_list = []
    for panel_index in range(order // panel_size):
        first = panel_index * panel_size
        last = first + panel_size
        diagonal_block = trailing[first:last, first:last]
        panel_lower = jnp.linalg.cholesky(diagonal_block)
        identity = jnp.eye(panel_size, dtype=jnp.float32)
        inverse = jax.scipy.linalg.solve_triangular(panel_lower, identity, lower=True)
        inverse_list.append(inverse)
        lower_factor = lower_factor.at[first:last, first:last].set(panel_lower)
        if last < order:
            below = jnp.dot(
                trailing[last:, first:last],
                inverse.T,
                precision=HIGHEST,
                preferred_element_type=jnp.float32,
            )
            lower_factor = lower_factor.at[last:, first:last].set(below)
            update = jnp.dot(below, below.T, precision=HIGHEST, preferred_element_type=jnp.float32)
            trailing = trailing.at[last:, last:].add(-update)
    return (lower_factor, inverse_list)


def cholesky_inverse(matrix, base_size):
    order = matrix.shape[0]
    if order <= base_size:
        return base_cholesky_inverse(matrix)
    half = order // 2
    lower_11, inverse_11 = cholesky_inverse(matrix[:half, :half], base_size)
    lower_21 = jnp.dot(matrix[half:, :half], inverse_11.T, precision=HIGH, preferred_element_type=jnp.float32)
    schur = matrix[half:, half:] - jnp.dot(lower_21, lower_21.T, precision=HIGH, preferred_element_type=jnp.float32)
    lower_22, inverse_22 = cholesky_inverse(schur, base_size)
    inverse_21 = -jnp.dot(
        inverse_22,
        jnp.dot(lower_21, inverse_11, precision=HIGH, preferred_element_type=jnp.float32),
        precision=HIGH,
        preferred_element_type=jnp.float32,
    )
    zero = jnp.zeros((half, half), jnp.float32)
    lower = jnp.block([[lower_11, zero], [lower_21, lower_22]])
    inverse = jnp.block([[inverse_11, zero], [inverse_21, inverse_22]])
    return (lower, inverse)


def border_solve(rows_in, lower_factor, inverse_list, panel_size):
    solved = []
    for panel_index in range(len(inverse_list)):
        first = panel_index * panel_size
        pending = rows_in[:, first : first + panel_size]
        for earlier in range(panel_index):
            coupling = lower_factor[
                first : first + panel_size, earlier * panel_size : (earlier + 1) * panel_size
            ]
            pending = pending - jnp.dot(
                solved[earlier], coupling.T, precision=HIGHEST, preferred_element_type=jnp.float32
            )
        solved.append(
            jnp.dot(
                pending,
                inverse_list[panel_index].T,
                precision=HIGHEST,
                preferred_element_type=jnp.float32,
            )
        )
    return jnp.concatenate(solved, axis=1)


def shards(child_update, block_map, obs_design, obs_target):
    inner_count = lax.axis_size("inner")
    group_count = lax.axis_size("outer")
    group_index = lax.axis_index("outer")
    member = lax.axis_index("inner")
    parent_count = (S + B) // BLK
    sep_rows = S // inner_count
    sep_blocks = S // BLK
    panel_size = min(S, 256)
    front_total = sum((group_count >> level_index + 1 for level_index in range(LEVELS)))
    target_total = front_total * sep_blocks
    row_count = obs_design.shape[0]
    step_rows = math.gcd(row_count, 256)
    target_ids = jnp.arange(target_total, dtype=jnp.int32)

    def add_rows(block_index, running):
        design = lax.dynamic_slice_in_dim(obs_design, block_index * step_rows, step_rows, 0)
        labels = lax.dynamic_slice_in_dim(obs_target, block_index * step_rows, step_rows, 0)
        selector = (labels[:, None] == target_ids[None, :]).astype(jnp.bfloat16)
        spread = selector[:, :, None] * design[:, None, :]
        return running + jnp.einsum(
            "rtj,rk->tjk", spread, design, preferred_element_type=jnp.float32
        )

    gram_blocks = lax.fori_loop(
        0, row_count // step_rows, add_rows, jnp.zeros((target_total, BLK, BLK), jnp.float32)
    )
    per_front = gram_blocks.reshape(front_total, S, BLK)
    half = group_index >> 2 & 1
    pair = group_index >> 1 & 1
    kept = jnp.concatenate(
        [
            lax.dynamic_slice_in_dim(per_front, 2 * half, 2, 0),
            lax.dynamic_slice_in_dim(per_front, 4 + half, 1, 0),
        ]
    )
    given = jnp.concatenate(
        [
            lax.dynamic_slice_in_dim(per_front, 2 - 2 * half, 2, 0),
            lax.dynamic_slice_in_dim(per_front, 5 - half, 1, 0),
        ]
    )
    kept = kept + partner_2(given, "outer", 2)
    given = jnp.stack([lax.dynamic_index_in_dim(kept, 1 - pair, 0, keepdims=False), kept[2]])
    arrived = partner_2(given, "outer", 1)
    kept = jnp.stack(
        [lax.dynamic_index_in_dim(kept, pair, 0, keepdims=False) + arrived[0], kept[2] + arrived[1]]
    )
    kept = kept + partner_2(kept, "outer", 0)
    obs_share = lax.psum_scatter(kept, "inner", scatter_dimension=1, tiled=True)
    current = child_update[0]
    pivot_list = []
    border_list = []
    front_offset = 0
    block_start = member * sep_rows // BLK * BLK
    for level_index in range(LEVELS):
        partner = group_index ^ 1 << level_index
        level_maps = block_map[level_index]
        own_map = lax.dynamic_index_in_dim(level_maps, group_index, 0, keepdims=False)
        sib_map = lax.dynamic_index_in_dim(level_maps, partner, 0, keepdims=False)
        sibling = partner_2(current, "outer", level_index)
        outgoing = jnp.stack(
            [
                owner_major(parent_columns(current, own_map, parent_count), inner_count),
                owner_major(parent_columns(sibling, sib_map, parent_count), inner_count),
            ]
        )
        arrived = lax.all_to_all(outgoing, "inner", split_axis=2, concat_axis=1, tiled=True)
        own_cols = parent_rows(arrived[0, :, 0, :], own_map, parent_count)
        sib_cols = parent_rows(arrived[1, :, 0, :], sib_map, parent_count)
        front_rows = (own_cols + sib_cols).T
        front_slot = front_offset + (group_index >> level_index + 1)
        obs_rows = obs_share[level_index]
        sep_front = front_rows[:sep_rows]
        block_now = lax.dynamic_slice_in_dim(sep_front, block_start, BLK, 1)
        sep_front = lax.dynamic_update_slice_in_dim(sep_front, block_now + obs_rows, block_start, 1)
        front_offset = front_offset + (group_count >> level_index + 1)
        pivot_all = lax.all_gather(sep_front[:, :S], "inner", axis=0, tiled=True)
        border_front = front_rows[sep_rows:]
        coupling_all = lax.all_gather(border_front[:, :S], "inner", axis=0, tiled=True)
        pivot_lower, pivot_inverse = cholesky_inverse(pivot_all, BLK)
        border_all = jnp.dot(
            coupling_all, pivot_inverse.T, precision=HIGH, preferred_element_type=jnp.float32
        )
        border_factor = lax.dynamic_slice_in_dim(border_all, member * (B // inner_count), B // inner_count, 0)
        product = jnp.einsum(
            "rs,cs->rc",
            border_factor,
            border_all,
            precision=HIGH,
            preferred_element_type=jnp.float32,
        )
        current = border_front[:, S:] - product
        pivot_list.append(lax.dynamic_slice_in_dim(pivot_lower, member * sep_rows, sep_rows, 0))
        border_list.append(border_factor)
    pivot_factor = jnp.stack(pivot_list)[:, None]
    border_out = jnp.stack(border_list)[:, None]
    return (pivot_factor, border_out, current[None])


def solution(mesh):
    in_specs = (P("outer", "inner", None), P(), P(("outer", "inner"), None), P(("outer", "inner")))
    out_specs = (
        P(None, "outer", "inner", None),
        P(None, "outer", "inner", None),
        P("outer", "inner", None),
    )
    return jax.shard_map(shards, mesh=mesh, in_specs=in_specs, out_specs=out_specs, check_vma=False)
```

```python
import math

import jax
import jax.numpy as jnp
from jax import lax
from jax.experimental import pallas as pl
from jax.experimental.pallas import tpu as pltpu
from jax.sharding import PartitionSpec as P

S = 1024
B = 2048
BLK = 128
LEVELS = 2


HIGHEST = lax.Precision.HIGHEST
HIGH = lax.Precision.HIGH
TILE = 8


def _kernel(a_ref, l_ref, x_ref, t_ref):
    n = a_ref.shape[0]
    tiles = n // TILE
    row = lax.broadcasted_iota(jnp.int32, (n, n), 0)
    col = lax.broadcasted_iota(jnp.int32, (n, n), 1)
    a = a_ref[...]
    t_ref[...] = jnp.where(row >= col, a, a.T)
    work = [t_ref[b * TILE : (b + 1) * TILE, :] for b in range(tiles)]
    sub = lax.broadcasted_iota(jnp.int32, (TILE, n), 0)
    lane = lax.broadcasted_iota(jnp.int32, (TILE, n), 1)
    lane1 = lax.broadcasted_iota(jnp.int32, (1, n), 1)
    sub1 = lax.broadcasted_iota(jnp.int32, (TILE, 1), 0)
    inv = [jnp.where(lane == sub + b * TILE, 1.0, 0.0).astype(jnp.float32) for b in range(tiles)]
    for c in range(n):
        first, i = divmod(c, TILE)
        ri = work[first][i : i + 1, :]
        s = lax.rsqrt(ri[:, c : c + 1])
        li = jnp.where(lane1 >= c, ri * s, 0.0)
        t_ref[c : c + 1, :] = li
        xi = inv[first][i : i + 1, :] * s
        for b in range(first, tiles):
            lk = work[b][:, c : c + 1] * s
            if b == first:
                lk = jnp.where(sub1 > i, lk, 0.0)
            work[b] = work[b] - lk * li
            if b == first:
                inv[b] = jnp.where(sub == i, xi, inv[b] - lk * xi)
            else:
                inv[b] = inv[b] - lk * xi
    for b in range(tiles):
        x_ref[b * TILE : (b + 1) * TILE, :] = inv[b]
    l_ref[...] = t_ref[...].T


def base_cholesky_inverse(a):
    n = a.shape[0]
    return pl.pallas_call(
        _kernel,
        out_shape=(jax.ShapeDtypeStruct((n, n), jnp.float32), jax.ShapeDtypeStruct((n, n), jnp.float32)),
        scratch_shapes=[pltpu.VMEM((n, n), jnp.float32)],
    )(a)


def partner_2(block, axis, bit):
    count = lax.axis_size(axis)
    route = []
    for low in range(count):
        high = low | 1 << bit
        if high != low and high < count:
            route += [(low, high), (high, low)]
    return lax.ppermute(block, axis, route)


def block_source(child_map, parent_count):
    child_count = child_map.shape[0]
    matches = child_map[:, None] == jnp.arange(parent_count, dtype=jnp.int32)[None, :]
    source = jnp.sum(
        jnp.where(matches, jnp.arange(child_count, dtype=jnp.int32)[:, None], 0), axis=0
    )
    present = jnp.any(matches, axis=0)
    return (source, present)


def parent_columns(child_rows, child_map, parent_count):
    row_count = child_rows.shape[0]
    child_count = child_map.shape[0]
    block_size = child_rows.shape[1] // child_count
    source, present = block_source(child_map, parent_count)
    blocks = child_rows.reshape(row_count, child_count, block_size)
    picked = jnp.take(blocks, source, axis=1)
    picked = jnp.where(present[None, :, None], picked, jnp.zeros_like(picked))
    return picked.reshape(row_count, parent_count * block_size)


def parent_rows(child_cols, child_map, parent_count):
    col_count = child_cols.shape[1]
    child_count = child_map.shape[0]
    block_size = child_cols.shape[0] // child_count
    source, present = block_source(child_map, parent_count)
    blocks = child_cols.reshape(child_count, block_size, col_count)
    picked = jnp.take(blocks, source, axis=0)
    picked = jnp.where(present[:, None, None], picked, jnp.zeros_like(picked))
    return picked.reshape(parent_count * block_size, col_count)


def owner_major(parent_cols, inner_count):
    row_count = parent_cols.shape[0]
    sep_part = parent_cols[:, :S].reshape(row_count, inner_count, S // inner_count)
    border_part = parent_cols[:, S:].reshape(row_count, inner_count, B // inner_count)
    return jnp.concatenate([sep_part, border_part], axis=2)


def blocked_cholesky(matrix, panel_size):
    order = matrix.shape[0]
    lower_factor = jnp.zeros_like(matrix)
    trailing = matrix
    inverse_list = []
    for panel_index in range(order // panel_size):
        first = panel_index * panel_size
        last = first + panel_size
        diagonal_block = trailing[first:last, first:last]
        panel_lower = jnp.linalg.cholesky(diagonal_block)
        identity = jnp.eye(panel_size, dtype=jnp.float32)
        inverse = jax.scipy.linalg.solve_triangular(panel_lower, identity, lower=True)
        inverse_list.append(inverse)
        lower_factor = lower_factor.at[first:last, first:last].set(panel_lower)
        if last < order:
            below = jnp.dot(
                trailing[last:, first:last],
                inverse.T,
                precision=HIGHEST,
                preferred_element_type=jnp.float32,
            )
            lower_factor = lower_factor.at[last:, first:last].set(below)
            update = jnp.dot(below, below.T, precision=HIGHEST, preferred_element_type=jnp.float32)
            trailing = trailing.at[last:, last:].add(-update)
    return (lower_factor, inverse_list)


def cholesky_inverse(matrix, base_size):
    order = matrix.shape[0]
    if order <= base_size:
        return base_cholesky_inverse(matrix)
    half = order // 2
    lower_11, inverse_11 = cholesky_inverse(matrix[:half, :half], base_size)
    lower_21 = jnp.dot(matrix[half:, :half], inverse_11.T, precision=HIGH, preferred_element_type=jnp.float32)
    schur = matrix[half:, half:] - jnp.dot(lower_21, lower_21.T, precision=HIGH, preferred_element_type=jnp.float32)
    lower_22, inverse_22 = cholesky_inverse(schur, base_size)
    inverse_21 = -jnp.dot(
        inverse_22,
        jnp.dot(lower_21, inverse_11, precision=HIGH, preferred_element_type=jnp.float32),
        precision=HIGH,
        preferred_element_type=jnp.float32,
    )
    zero = jnp.zeros((half, half), jnp.float32)
    lower = jnp.block([[lower_11, zero], [lower_21, lower_22]])
    inverse = jnp.block([[inverse_11, zero], [inverse_21, inverse_22]])
    return (lower, inverse)


def border_solve(rows_in, lower_factor, inverse_list, panel_size):
    solved = []
    for panel_index in range(len(inverse_list)):
        first = panel_index * panel_size
        pending = rows_in[:, first : first + panel_size]
        for earlier in range(panel_index):
            coupling = lower_factor[
                first : first + panel_size, earlier * panel_size : (earlier + 1) * panel_size
            ]
            pending = pending - jnp.dot(
                solved[earlier], coupling.T, precision=HIGHEST, preferred_element_type=jnp.float32
            )
        solved.append(
            jnp.dot(
                pending,
                inverse_list[panel_index].T,
                precision=HIGHEST,
                preferred_element_type=jnp.float32,
            )
        )
    return jnp.concatenate(solved, axis=1)


def shards(child_update, block_map, obs_design, obs_target):
    inner_count = lax.axis_size("inner")
    group_count = lax.axis_size("outer")
    group_index = lax.axis_index("outer")
    member = lax.axis_index("inner")
    parent_count = (S + B) // BLK
    sep_rows = S // inner_count
    sep_blocks = S // BLK
    panel_size = min(S, 256)
    front_total = sum((group_count >> level_index + 1 for level_index in range(LEVELS)))
    target_total = front_total * sep_blocks
    row_count = obs_design.shape[0]
    step_rows = math.gcd(row_count, 256)
    target_ids = jnp.arange(target_total, dtype=jnp.int32)

    def add_rows(block_index, running):
        design = lax.dynamic_slice_in_dim(obs_design, block_index * step_rows, step_rows, 0)
        labels = lax.dynamic_slice_in_dim(obs_target, block_index * step_rows, step_rows, 0)
        selector = (labels[:, None] == target_ids[None, :]).astype(jnp.bfloat16)
        spread = selector[:, :, None] * design[:, None, :]
        return running + jnp.einsum(
            "rtj,rk->tjk", spread, design, preferred_element_type=jnp.float32
        )

    gram_blocks = lax.fori_loop(
        0, row_count // step_rows, add_rows, jnp.zeros((target_total, BLK, BLK), jnp.float32)
    )
    per_front = gram_blocks.reshape(front_total, S, BLK)
    obs_share = lax.psum_scatter(per_front, "inner", scatter_dimension=1, tiled=True)
    for bit in range(group_count.bit_length() - 1):
        obs_share = obs_share + partner_2(obs_share, "outer", bit)
    current = child_update[0]
    pivot_list = []
    border_list = []
    front_offset = 0
    block_start = member * sep_rows // BLK * BLK
    for level_index in range(LEVELS):
        partner = group_index ^ 1 << level_index
        level_maps = block_map[level_index]
        own_map = lax.dynamic_index_in_dim(level_maps, group_index, 0, keepdims=False)
        sib_map = lax.dynamic_index_in_dim(level_maps, partner, 0, keepdims=False)
        sibling = partner_2(current, "outer", level_index)
        outgoing = jnp.stack(
            [
                owner_major(parent_columns(current, own_map, parent_count), inner_count),
                owner_major(parent_columns(sibling, sib_map, parent_count), inner_count),
            ]
        )
        arrived = lax.all_to_all(outgoing, "inner", split_axis=2, concat_axis=1, tiled=True)
        own_cols = parent_rows(arrived[0, :, 0, :], own_map, parent_count)
        sib_cols = parent_rows(arrived[1, :, 0, :], sib_map, parent_count)
        front_rows = (own_cols + sib_cols).T
        front_slot = front_offset + (group_index >> level_index + 1)
        obs_rows = lax.dynamic_index_in_dim(obs_share, front_slot, 0, keepdims=False)
        sep_front = front_rows[:sep_rows]
        block_now = lax.dynamic_slice_in_dim(sep_front, block_start, BLK, 1)
        sep_front = lax.dynamic_update_slice_in_dim(sep_front, block_now + obs_rows, block_start, 1)
        front_offset = front_offset + (group_count >> level_index + 1)
        pivot_all = lax.all_gather(sep_front[:, :S], "inner", axis=0, tiled=True)
        border_front = front_rows[sep_rows:]
        coupling_all = lax.all_gather(border_front[:, :S], "inner", axis=0, tiled=True)
        pivot_lower, pivot_inverse = cholesky_inverse(pivot_all, BLK)
        border_all = jnp.dot(
            coupling_all, pivot_inverse.T, precision=HIGH, preferred_element_type=jnp.float32
        )
        border_factor = lax.dynamic_slice_in_dim(border_all, member * (B // inner_count), B // inner_count, 0)
        product = jnp.einsum(
            "rs,cs->rc",
            border_factor,
            border_all,
            precision=HIGH,
            preferred_element_type=jnp.float32,
        )
        current = border_front[:, S:] - product
        pivot_list.append(lax.dynamic_slice_in_dim(pivot_lower, member * sep_rows, sep_rows, 0))
        border_list.append(border_factor)
    pivot_factor = jnp.stack(pivot_list)[:, None]
    border_out = jnp.stack(border_list)[:, None]
    return (pivot_factor, border_out, current[None])


def solution(mesh):
    in_specs = (P("outer", "inner", None), P(), P(("outer", "inner"), None), P(("outer", "inner")))
    out_specs = (
        P(None, "outer", "inner", None),
        P(None, "outer", "inner", None),
        P("outer", "inner", None),
    )
    return jax.shard_map(shards, mesh=mesh, in_specs=in_specs, out_specs=out_specs, check_vma=False)
```

```python
import math

import jax
import jax.numpy as jnp
from jax import lax
from jax.experimental import pallas as pl
from jax.experimental.pallas import tpu as pltpu
from jax.sharding import PartitionSpec as P

S = 1024
B = 2048
BLK = 128
LEVELS = 2


HIGHEST = lax.Precision.HIGHEST
HIGH = lax.Precision.HIGH
TILE = 8


def _kernel(a_ref, l_ref, x_ref, t_ref):
    n = a_ref.shape[0]
    tiles = n // TILE
    row = lax.broadcasted_iota(jnp.int32, (n, n), 0)
    col = lax.broadcasted_iota(jnp.int32, (n, n), 1)
    a = a_ref[...]
    t_ref[...] = jnp.where(row >= col, a, a.T)
    work = [t_ref[b * TILE : (b + 1) * TILE, :] for b in range(tiles)]
    sub = lax.broadcasted_iota(jnp.int32, (TILE, n), 0)
    lane = lax.broadcasted_iota(jnp.int32, (TILE, n), 1)
    lane1 = lax.broadcasted_iota(jnp.int32, (1, n), 1)
    sub1 = lax.broadcasted_iota(jnp.int32, (TILE, 1), 0)
    inv = [jnp.where(lane == sub + b * TILE, 1.0, 0.0).astype(jnp.float32) for b in range(tiles)]
    for c in range(n):
        first, i = divmod(c, TILE)
        ri = work[first][i : i + 1, :]
        s = lax.rsqrt(ri[:, c : c + 1])
        li = jnp.where(lane1 >= c, ri * s, 0.0)
        t_ref[c : c + 1, :] = li
        xi = inv[first][i : i + 1, :] * s
        for b in range(first, tiles):
            lk = work[b][:, c : c + 1] * s
            if b == first:
                lk = jnp.where(sub1 > i, lk, 0.0)
            work[b] = work[b] - lk * li
            if b == first:
                inv[b] = jnp.where(sub == i, xi, inv[b] - lk * xi)
            else:
                inv[b] = inv[b] - lk * xi
    for b in range(tiles):
        x_ref[b * TILE : (b + 1) * TILE, :] = inv[b]
    l_ref[...] = t_ref[...].T


def base_cholesky_inverse(a):
    n = a.shape[0]
    return pl.pallas_call(
        _kernel,
        out_shape=(jax.ShapeDtypeStruct((n, n), jnp.float32), jax.ShapeDtypeStruct((n, n), jnp.float32)),
        scratch_shapes=[pltpu.VMEM((n, n), jnp.float32)],
    )(a)


def partner_2(block, axis, bit):
    count = lax.axis_size(axis)
    route = []
    for low in range(count):
        high = low | 1 << bit
        if high != low and high < count:
            route += [(low, high), (high, low)]
    return lax.ppermute(block, axis, route)


def block_source(child_map, parent_count):
    child_count = child_map.shape[0]
    matches = child_map[:, None] == jnp.arange(parent_count, dtype=jnp.int32)[None, :]
    source = jnp.sum(
        jnp.where(matches, jnp.arange(child_count, dtype=jnp.int32)[:, None], 0), axis=0
    )
    present = jnp.any(matches, axis=0)
    return (source, present)


def parent_columns(child_rows, child_map, parent_count):
    row_count = child_rows.shape[0]
    child_count = child_map.shape[0]
    block_size = child_rows.shape[1] // child_count
    source, present = block_source(child_map, parent_count)
    blocks = child_rows.reshape(row_count, child_count, block_size)
    picked = jnp.take(blocks, source, axis=1)
    picked = jnp.where(present[None, :, None], picked, jnp.zeros_like(picked))
    return picked.reshape(row_count, parent_count * block_size)


def parent_rows(child_cols, child_map, parent_count):
    col_count = child_cols.shape[1]
    child_count = child_map.shape[0]
    block_size = child_cols.shape[0] // child_count
    source, present = block_source(child_map, parent_count)
    blocks = child_cols.reshape(child_count, block_size, col_count)
    picked = jnp.take(blocks, source, axis=0)
    picked = jnp.where(present[:, None, None], picked, jnp.zeros_like(picked))
    return picked.reshape(parent_count * block_size, col_count)


def owner_major(parent_cols, inner_count):
    row_count = parent_cols.shape[0]
    sep_part = parent_cols[:, :S].reshape(row_count, inner_count, S // inner_count)
    border_part = parent_cols[:, S:].reshape(row_count, inner_count, B // inner_count)
    return jnp.concatenate([sep_part, border_part], axis=2)


def blocked_cholesky(matrix, panel_size):
    order = matrix.shape[0]
    lower_factor = jnp.zeros_like(matrix)
    trailing = matrix
    inverse_list = []
    for panel_index in range(order // panel_size):
        first = panel_index * panel_size
        last = first + panel_size
        diagonal_block = trailing[first:last, first:last]
        panel_lower = jnp.linalg.cholesky(diagonal_block)
        identity = jnp.eye(panel_size, dtype=jnp.float32)
        inverse = jax.scipy.linalg.solve_triangular(panel_lower, identity, lower=True)
        inverse_list.append(inverse)
        lower_factor = lower_factor.at[first:last, first:last].set(panel_lower)
        if last < order:
            below = jnp.dot(
                trailing[last:, first:last],
                inverse.T,
                precision=HIGHEST,
                preferred_element_type=jnp.float32,
            )
            lower_factor = lower_factor.at[last:, first:last].set(below)
            update = jnp.dot(below, below.T, precision=HIGHEST, preferred_element_type=jnp.float32)
            trailing = trailing.at[last:, last:].add(-update)
    return (lower_factor, inverse_list)


def cholesky_inverse(matrix, base_size):
    order = matrix.shape[0]
    if order <= base_size:
        return base_cholesky_inverse(matrix)
    half = order // 2
    lower_11, inverse_11 = cholesky_inverse(matrix[:half, :half], base_size)
    lower_21 = jnp.dot(matrix[half:, :half], inverse_11.T, precision=HIGH, preferred_element_type=jnp.float32)
    schur = matrix[half:, half:] - jnp.dot(lower_21, lower_21.T, precision=HIGH, preferred_element_type=jnp.float32)
    lower_22, inverse_22 = cholesky_inverse(schur, base_size)
    inverse_21 = -jnp.dot(
        inverse_22,
        jnp.dot(lower_21, inverse_11, precision=HIGH, preferred_element_type=jnp.float32),
        precision=HIGH,
        preferred_element_type=jnp.float32,
    )
    zero = jnp.zeros((half, half), jnp.float32)
    lower = jnp.block([[lower_11, zero], [lower_21, lower_22]])
    inverse = jnp.block([[inverse_11, zero], [inverse_21, inverse_22]])
    return (lower, inverse)


def border_solve(rows_in, lower_factor, inverse_list, panel_size):
    solved = []
    for panel_index in range(len(inverse_list)):
        first = panel_index * panel_size
        pending = rows_in[:, first : first + panel_size]
        for earlier in range(panel_index):
            coupling = lower_factor[
                first : first + panel_size, earlier * panel_size : (earlier + 1) * panel_size
            ]
            pending = pending - jnp.dot(
                solved[earlier], coupling.T, precision=HIGHEST, preferred_element_type=jnp.float32
            )
        solved.append(
            jnp.dot(
                pending,
                inverse_list[panel_index].T,
                precision=HIGHEST,
                preferred_element_type=jnp.float32,
            )
        )
    return jnp.concatenate(solved, axis=1)


def shards(child_update, block_map, obs_design, obs_target):
    inner_count = lax.axis_size("inner")
    group_count = lax.axis_size("outer")
    group_index = lax.axis_index("outer")
    member = lax.axis_index("inner")
    parent_count = (S + B) // BLK
    sep_rows = S // inner_count
    sep_blocks = S // BLK
    panel_size = min(S, 256)
    front_total = sum((group_count >> level_index + 1 for level_index in range(LEVELS)))
    target_total = front_total * sep_blocks
    row_count = obs_design.shape[0]
    step_rows = math.gcd(row_count, 256)
    target_ids = jnp.arange(target_total, dtype=jnp.int32)

    def add_rows(block_index, running):
        design = lax.dynamic_slice_in_dim(obs_design, block_index * step_rows, step_rows, 0)
        labels = lax.dynamic_slice_in_dim(obs_target, block_index * step_rows, step_rows, 0)
        selector = (labels[:, None] == target_ids[None, :]).astype(jnp.bfloat16)
        spread = selector[:, :, None] * design[:, None, :]
        return running + jnp.einsum(
            "rtj,rk->tjk", spread, design, preferred_element_type=jnp.float32
        )

    gram_blocks = lax.fori_loop(
        0, row_count // step_rows, add_rows, jnp.zeros((target_total, BLK, BLK), jnp.float32)
    )
    per_front = gram_blocks.reshape(front_total, S, BLK)
    obs_share = lax.psum_scatter(per_front, "inner", scatter_dimension=1, tiled=True)
    for bit in range(group_count.bit_length() - 1):
        obs_share = obs_share + partner_2(obs_share, "outer", bit)
    current = child_update[0]
    pivot_list = []
    border_list = []
    front_offset = 0
    block_start = member * sep_rows // BLK * BLK
    for level_index in range(LEVELS):
        partner = group_index ^ 1 << level_index
        level_maps = block_map[level_index]
        own_map = lax.dynamic_index_in_dim(level_maps, group_index, 0, keepdims=False)
        sib_map = lax.dynamic_index_in_dim(level_maps, partner, 0, keepdims=False)
        sibling = partner_2(current, "outer", level_index)
        outgoing = jnp.stack(
            [
                owner_major(parent_columns(current, own_map, parent_count), inner_count),
                owner_major(parent_columns(sibling, sib_map, parent_count), inner_count),
            ]
        )
        arrived = lax.all_to_all(outgoing, "inner", split_axis=2, concat_axis=1, tiled=True)
        own_cols = parent_rows(arrived[0, :, 0, :], own_map, parent_count)
        sib_cols = parent_rows(arrived[1, :, 0, :], sib_map, parent_count)
        front_rows = (own_cols + sib_cols).T
        front_slot = front_offset + (group_index >> level_index + 1)
        obs_rows = lax.dynamic_index_in_dim(obs_share, front_slot, 0, keepdims=False)
        sep_front = front_rows[:sep_rows]
        block_now = lax.dynamic_slice_in_dim(sep_front, block_start, BLK, 1)
        sep_front = lax.dynamic_update_slice_in_dim(sep_front, block_now + obs_rows, block_start, 1)
        front_offset = front_offset + (group_count >> level_index + 1)
        pivot_all = lax.all_gather(sep_front[:, :S], "inner", axis=0, tiled=True)
        border_front = front_rows[sep_rows:]
        coupling_all = lax.all_gather(border_front[:, :S], "inner", axis=0, tiled=True)
        half = S // 2
        lower_11, inverse_11 = cholesky_inverse(pivot_all[:half, :half], BLK)
        lower_21 = jnp.dot(
            pivot_all[half:, :half], inverse_11.T, precision=HIGH, preferred_element_type=jnp.float32
        )
        schur = pivot_all[half:, half:] - jnp.dot(
            lower_21, lower_21.T, precision=HIGH, preferred_element_type=jnp.float32
        )
        lower_22, inverse_22 = cholesky_inverse(schur, BLK)
        inverse_21 = -jnp.dot(
            inverse_22,
            jnp.dot(lower_21, inverse_11, precision=HIGH, preferred_element_type=jnp.float32),
            precision=HIGH,
            preferred_element_type=jnp.float32,
        )
        zero = jnp.zeros((half, half), jnp.float32)
        pivot_lower = jnp.block([[lower_11, zero], [lower_21, lower_22]])
        border_left = jnp.dot(
            coupling_all[:, :half], inverse_11.T, precision=HIGH, preferred_element_type=jnp.float32
        )
        border_right = jnp.dot(
            coupling_all[:, :half], inverse_21.T, precision=HIGH, preferred_element_type=jnp.float32
        ) + jnp.dot(
            coupling_all[:, half:], inverse_22.T, precision=HIGH, preferred_element_type=jnp.float32
        )
        own_rows = B // inner_count
        own_left = lax.dynamic_slice_in_dim(border_left, member * own_rows, own_rows, 0)
        own_right = lax.dynamic_slice_in_dim(border_right, member * own_rows, own_rows, 0)
        border_factor = jnp.concatenate([own_left, own_right], axis=1)
        product = jnp.einsum(
            "rs,cs->rc", own_left, border_left, precision=HIGH, preferred_element_type=jnp.float32
        ) + jnp.einsum(
            "rs,cs->rc", own_right, border_right, precision=HIGH, preferred_element_type=jnp.float32
        )
        current = border_front[:, S:] - product
        pivot_list.append(lax.dynamic_slice_in_dim(pivot_lower, member * sep_rows, sep_rows, 0))
        border_list.append(border_factor)
    pivot_factor = jnp.stack(pivot_list)[:, None]
    border_out = jnp.stack(border_list)[:, None]
    return (pivot_factor, border_out, current[None])


def solution(mesh):
    in_specs = (P("outer", "inner", None), P(), P(("outer", "inner"), None), P(("outer", "inner")))
    out_specs = (
        P(None, "outer", "inner", None),
        P(None, "outer", "inner", None),
        P("outer", "inner", None),
    )
    return jax.shard_map(shards, mesh=mesh, in_specs=in_specs, out_specs=out_specs, check_vma=False)
```

```python
import math

import jax
import jax.numpy as jnp
from jax import lax
from jax.experimental import pallas as pl
from jax.experimental.pallas import tpu as pltpu
from jax.sharding import PartitionSpec as P

S = 1024
B = 2048
BLK = 128
LEVELS = 2


HIGHEST = lax.Precision.HIGHEST
HIGH = lax.Precision.HIGH
TILE = 8


def _kernel(a_ref, l_ref, x_ref, t_ref):
    n = a_ref.shape[0]
    tiles = n // TILE
    row = lax.broadcasted_iota(jnp.int32, (n, n), 0)
    col = lax.broadcasted_iota(jnp.int32, (n, n), 1)
    a = a_ref[...]
    t_ref[...] = jnp.where(row >= col, a, a.T)
    work = [t_ref[b * TILE : (b + 1) * TILE, :] for b in range(tiles)]
    sub = lax.broadcasted_iota(jnp.int32, (TILE, n), 0)
    lane = lax.broadcasted_iota(jnp.int32, (TILE, n), 1)
    lane1 = lax.broadcasted_iota(jnp.int32, (1, n), 1)
    sub1 = lax.broadcasted_iota(jnp.int32, (TILE, 1), 0)
    inv = [jnp.where(lane == sub + b * TILE, 1.0, 0.0).astype(jnp.float32) for b in range(tiles)]
    for c in range(n):
        first, i = divmod(c, TILE)
        ri = work[first][i : i + 1, :]
        s = lax.rsqrt(ri[:, c : c + 1])
        li = jnp.where(lane1 >= c, ri * s, 0.0)
        t_ref[c : c + 1, :] = li
        xi = inv[first][i : i + 1, :] * s
        for b in range(first, tiles):
            lk = work[b][:, c : c + 1] * s
            if b == first:
                lk = jnp.where(sub1 > i, lk, 0.0)
            work[b] = work[b] - lk * li
            if b == first:
                inv[b] = jnp.where(sub == i, xi, inv[b] - lk * xi)
            else:
                inv[b] = inv[b] - lk * xi
    for b in range(tiles):
        x_ref[b * TILE : (b + 1) * TILE, :] = inv[b]
    l_ref[...] = t_ref[...].T


def base_cholesky_inverse(a):
    n = a.shape[0]
    return pl.pallas_call(
        _kernel,
        out_shape=(jax.ShapeDtypeStruct((n, n), jnp.float32), jax.ShapeDtypeStruct((n, n), jnp.float32)),
        scratch_shapes=[pltpu.VMEM((n, n), jnp.float32)],
    )(a)


def partner_2(block, axis, bit):
    count = lax.axis_size(axis)
    route = []
    for low in range(count):
        high = low | 1 << bit
        if high != low and high < count:
            route += [(low, high), (high, low)]
    return lax.ppermute(block, axis, route)


def block_source(child_map, parent_count):
    child_count = child_map.shape[0]
    matches = child_map[:, None] == jnp.arange(parent_count, dtype=jnp.int32)[None, :]
    source = jnp.sum(
        jnp.where(matches, jnp.arange(child_count, dtype=jnp.int32)[:, None], 0), axis=0
    )
    present = jnp.any(matches, axis=0)
    return (source, present)


def parent_columns(child_rows, child_map, parent_count):
    row_count = child_rows.shape[0]
    child_count = child_map.shape[0]
    block_size = child_rows.shape[1] // child_count
    source, present = block_source(child_map, parent_count)
    blocks = child_rows.reshape(row_count, child_count, block_size)
    picked = jnp.take(blocks, source, axis=1)
    picked = jnp.where(present[None, :, None], picked, jnp.zeros_like(picked))
    return picked.reshape(row_count, parent_count * block_size)


def parent_rows(child_cols, child_map, parent_count):
    col_count = child_cols.shape[1]
    child_count = child_map.shape[0]
    block_size = child_cols.shape[0] // child_count
    source, present = block_source(child_map, parent_count)
    blocks = child_cols.reshape(child_count, block_size, col_count)
    picked = jnp.take(blocks, source, axis=0)
    picked = jnp.where(present[:, None, None], picked, jnp.zeros_like(picked))
    return picked.reshape(parent_count * block_size, col_count)


def owner_major(parent_cols, inner_count):
    row_count = parent_cols.shape[0]
    sep_part = parent_cols[:, :S].reshape(row_count, inner_count, S // inner_count)
    border_part = parent_cols[:, S:].reshape(row_count, inner_count, B // inner_count)
    return jnp.concatenate([sep_part, border_part], axis=2)


def blocked_cholesky(matrix, panel_size):
    order = matrix.shape[0]
    lower_factor = jnp.zeros_like(matrix)
    trailing = matrix
    inverse_list = []
    for panel_index in range(order // panel_size):
        first = panel_index * panel_size
        last = first + panel_size
        diagonal_block = trailing[first:last, first:last]
        panel_lower = jnp.linalg.cholesky(diagonal_block)
        identity = jnp.eye(panel_size, dtype=jnp.float32)
        inverse = jax.scipy.linalg.solve_triangular(panel_lower, identity, lower=True)
        inverse_list.append(inverse)
        lower_factor = lower_factor.at[first:last, first:last].set(panel_lower)
        if last < order:
            below = jnp.dot(
                trailing[last:, first:last],
                inverse.T,
                precision=HIGHEST,
                preferred_element_type=jnp.float32,
            )
            lower_factor = lower_factor.at[last:, first:last].set(below)
            update = jnp.dot(below, below.T, precision=HIGHEST, preferred_element_type=jnp.float32)
            trailing = trailing.at[last:, last:].add(-update)
    return (lower_factor, inverse_list)


def cholesky_inverse(matrix, base_size):
    order = matrix.shape[0]
    if order <= base_size:
        return base_cholesky_inverse(matrix)
    half = order // 2
    lower_11, inverse_11 = cholesky_inverse(matrix[:half, :half], base_size)
    lower_21 = jnp.dot(matrix[half:, :half], inverse_11.T, precision=HIGH, preferred_element_type=jnp.float32)
    schur = matrix[half:, half:] - jnp.dot(lower_21, lower_21.T, precision=HIGH, preferred_element_type=jnp.float32)
    lower_22, inverse_22 = cholesky_inverse(schur, base_size)
    inverse_21 = -jnp.dot(
        inverse_22,
        jnp.dot(lower_21, inverse_11, precision=HIGH, preferred_element_type=jnp.float32),
        precision=HIGH,
        preferred_element_type=jnp.float32,
    )
    zero = jnp.zeros((half, half), jnp.float32)
    lower = jnp.block([[lower_11, zero], [lower_21, lower_22]])
    inverse = jnp.block([[inverse_11, zero], [inverse_21, inverse_22]])
    return (lower, inverse)


def border_solve(rows_in, lower_factor, inverse_list, panel_size):
    solved = []
    for panel_index in range(len(inverse_list)):
        first = panel_index * panel_size
        pending = rows_in[:, first : first + panel_size]
        for earlier in range(panel_index):
            coupling = lower_factor[
                first : first + panel_size, earlier * panel_size : (earlier + 1) * panel_size
            ]
            pending = pending - jnp.dot(
                solved[earlier], coupling.T, precision=HIGHEST, preferred_element_type=jnp.float32
            )
        solved.append(
            jnp.dot(
                pending,
                inverse_list[panel_index].T,
                precision=HIGHEST,
                preferred_element_type=jnp.float32,
            )
        )
    return jnp.concatenate(solved, axis=1)


def shards(child_update, block_map, obs_design, obs_target):
    inner_count = lax.axis_size("inner")
    group_count = lax.axis_size("outer")
    group_index = lax.axis_index("outer")
    member = lax.axis_index("inner")
    parent_count = (S + B) // BLK
    sep_rows = S // inner_count
    sep_blocks = S // BLK
    panel_size = min(S, 256)
    front_total = sum((group_count >> level_index + 1 for level_index in range(LEVELS)))
    target_total = front_total * sep_blocks
    row_count = obs_design.shape[0]
    step_rows = math.gcd(row_count, 256)
    target_ids = jnp.arange(target_total, dtype=jnp.int32)

    def add_rows(block_index, running):
        design = lax.dynamic_slice_in_dim(obs_design, block_index * step_rows, step_rows, 0)
        labels = lax.dynamic_slice_in_dim(obs_target, block_index * step_rows, step_rows, 0)
        selector = (labels[:, None] == target_ids[None, :]).astype(jnp.bfloat16)
        spread = selector[:, :, None] * design[:, None, :]
        return running + jnp.einsum(
            "rtj,rk->tjk", spread, design, preferred_element_type=jnp.float32
        )

    gram_blocks = lax.fori_loop(
        0, row_count // step_rows, add_rows, jnp.zeros((target_total, BLK, BLK), jnp.float32)
    )
    gram_parts = gram_blocks.reshape(front_total, inner_count, sep_rows, BLK).transpose(1, 0, 2, 3)
    gram_parts = gram_parts.reshape(inner_count, -1)
    current = child_update[0]
    pivot_list = []
    border_list = []
    front_offset = 0
    block_start = member * sep_rows // BLK * BLK
    for level_index in range(LEVELS):
        partner = group_index ^ 1 << level_index
        level_maps = block_map[level_index]
        own_map = lax.dynamic_index_in_dim(level_maps, group_index, 0, keepdims=False)
        sib_map = lax.dynamic_index_in_dim(level_maps, partner, 0, keepdims=False)
        sibling = partner_2(current, "outer", level_index)
        outgoing = jnp.stack(
            [
                owner_major(parent_columns(current, own_map, parent_count), inner_count),
                owner_major(parent_columns(sibling, sib_map, parent_count), inner_count),
            ]
        )
        if level_index == 0:
            front_parts = outgoing.transpose(2, 0, 1, 3).reshape(inner_count, -1)
            front_size = front_parts.shape[1]
            both = lax.all_to_all(
                jnp.concatenate([front_parts, gram_parts], axis=1), "inner", 0, 0, tiled=True
            )
            arrived = both[:, :front_size].reshape(inner_count, 2, B // inner_count, 1, outgoing.shape[3])
            arrived = arrived.transpose(1, 0, 2, 3, 4).reshape(2, B, 1, outgoing.shape[3])
            obs_share = jnp.sum(
                both[:, front_size:].reshape(inner_count, front_total, sep_rows, BLK), axis=0
            )
            for bit in range(group_count.bit_length() - 1):
                obs_share = obs_share + partner_2(obs_share, "outer", bit)
        else:
            arrived = lax.all_to_all(outgoing, "inner", split_axis=2, concat_axis=1, tiled=True)
        own_cols = parent_rows(arrived[0, :, 0, :], own_map, parent_count)
        sib_cols = parent_rows(arrived[1, :, 0, :], sib_map, parent_count)
        front_rows = (own_cols + sib_cols).T
        front_slot = front_offset + (group_index >> level_index + 1)
        obs_rows = lax.dynamic_index_in_dim(obs_share, front_slot, 0, keepdims=False)
        sep_front = front_rows[:sep_rows]
        block_now = lax.dynamic_slice_in_dim(sep_front, block_start, BLK, 1)
        sep_front = lax.dynamic_update_slice_in_dim(sep_front, block_now + obs_rows, block_start, 1)
        front_offset = front_offset + (group_count >> level_index + 1)
        pivot_all = lax.all_gather(sep_front[:, :S], "inner", axis=0, tiled=True)
        border_front = front_rows[sep_rows:]
        coupling_all = lax.all_gather(border_front[:, :S], "inner", axis=0, tiled=True)
        half = S // 2
        lower_11, inverse_11 = cholesky_inverse(pivot_all[:half, :half], BLK)
        lower_21 = jnp.dot(
            pivot_all[half:, :half], inverse_11.T, precision=HIGH, preferred_element_type=jnp.float32
        )
        schur = pivot_all[half:, half:] - jnp.dot(
            lower_21, lower_21.T, precision=HIGH, preferred_element_type=jnp.float32
        )
        lower_22, inverse_22 = cholesky_inverse(schur, BLK)
        inverse_21 = -jnp.dot(
            inverse_22,
            jnp.dot(lower_21, inverse_11, precision=HIGH, preferred_element_type=jnp.float32),
            precision=HIGH,
            preferred_element_type=jnp.float32,
        )
        zero = jnp.zeros((half, half), jnp.float32)
        pivot_lower = jnp.block([[lower_11, zero], [lower_21, lower_22]])
        border_left = jnp.dot(
            coupling_all[:, :half], inverse_11.T, precision=HIGH, preferred_element_type=jnp.float32
        )
        border_right = jnp.dot(
            coupling_all[:, :half], inverse_21.T, precision=HIGH, preferred_element_type=jnp.float32
        ) + jnp.dot(
            coupling_all[:, half:], inverse_22.T, precision=HIGH, preferred_element_type=jnp.float32
        )
        own_rows = B // inner_count
        own_left = lax.dynamic_slice_in_dim(border_left, member * own_rows, own_rows, 0)
        own_right = lax.dynamic_slice_in_dim(border_right, member * own_rows, own_rows, 0)
        border_factor = jnp.concatenate([own_left, own_right], axis=1)
        product = jnp.einsum(
            "rs,cs->rc", own_left, border_left, precision=HIGH, preferred_element_type=jnp.float32
        ) + jnp.einsum(
            "rs,cs->rc", own_right, border_right, precision=HIGH, preferred_element_type=jnp.float32
        )
        current = border_front[:, S:] - product
        pivot_list.append(lax.dynamic_slice_in_dim(pivot_lower, member * sep_rows, sep_rows, 0))
        border_list.append(border_factor)
    pivot_factor = jnp.stack(pivot_list)[:, None]
    border_out = jnp.stack(border_list)[:, None]
    return (pivot_factor, border_out, current[None])


def solution(mesh):
    in_specs = (P("outer", "inner", None), P(), P(("outer", "inner"), None), P(("outer", "inner")))
    out_specs = (
        P(None, "outer", "inner", None),
        P(None, "outer", "inner", None),
        P("outer", "inner", None),
    )
    return jax.shard_map(shards, mesh=mesh, in_specs=in_specs, out_specs=out_specs, check_vma=False)
```

```python
import math

import jax
import jax.numpy as jnp
from jax import lax
from jax.experimental import pallas as pl
from jax.experimental.pallas import tpu as pltpu
from jax.sharding import PartitionSpec as P

S = 1024
B = 2048
BLK = 128
LEVELS = 2


HIGHEST = lax.Precision.HIGHEST
HIGH = lax.Precision.HIGH
TILE = 8


def _kernel(a_ref, l_ref, x_ref, t_ref):
    n = a_ref.shape[0]
    tiles = n // TILE
    row = lax.broadcasted_iota(jnp.int32, (n, n), 0)
    col = lax.broadcasted_iota(jnp.int32, (n, n), 1)
    a = a_ref[...]
    t_ref[...] = jnp.where(row >= col, a, a.T)
    work = [t_ref[b * TILE : (b + 1) * TILE, :] for b in range(tiles)]
    sub = lax.broadcasted_iota(jnp.int32, (TILE, n), 0)
    lane = lax.broadcasted_iota(jnp.int32, (TILE, n), 1)
    lane1 = lax.broadcasted_iota(jnp.int32, (1, n), 1)
    sub1 = lax.broadcasted_iota(jnp.int32, (TILE, 1), 0)
    inv = [jnp.where(lane == sub + b * TILE, 1.0, 0.0).astype(jnp.float32) for b in range(tiles)]
    for c in range(n):
        first, i = divmod(c, TILE)
        ri = work[first][i : i + 1, :]
        s = lax.rsqrt(ri[:, c : c + 1])
        li = jnp.where(lane1 >= c, ri * s, 0.0)
        t_ref[c : c + 1, :] = li
        xi = inv[first][i : i + 1, :] * s
        for b in range(first, tiles):
            lk = work[b][:, c : c + 1] * s
            if b == first:
                lk = jnp.where(sub1 > i, lk, 0.0)
            work[b] = work[b] - lk * li
            if b == first:
                inv[b] = jnp.where(sub == i, xi, inv[b] - lk * xi)
            else:
                inv[b] = inv[b] - lk * xi
    for b in range(tiles):
        x_ref[b * TILE : (b + 1) * TILE, :] = inv[b]
    l_ref[...] = t_ref[...].T


def base_cholesky_inverse(a):
    n = a.shape[0]
    return pl.pallas_call(
        _kernel,
        out_shape=(jax.ShapeDtypeStruct((n, n), jnp.float32), jax.ShapeDtypeStruct((n, n), jnp.float32)),
        scratch_shapes=[pltpu.VMEM((n, n), jnp.float32)],
    )(a)


def partner_2(block, axis, bit):
    count = lax.axis_size(axis)
    route = []
    for low in range(count):
        high = low | 1 << bit
        if high != low and high < count:
            route += [(low, high), (high, low)]
    return lax.ppermute(block, axis, route)


def block_source(child_map, parent_count):
    child_count = child_map.shape[0]
    matches = child_map[:, None] == jnp.arange(parent_count, dtype=jnp.int32)[None, :]
    source = jnp.sum(
        jnp.where(matches, jnp.arange(child_count, dtype=jnp.int32)[:, None], 0), axis=0
    )
    present = jnp.any(matches, axis=0)
    return (source, present)


def parent_columns(child_rows, child_map, parent_count):
    row_count = child_rows.shape[0]
    child_count = child_map.shape[0]
    block_size = child_rows.shape[1] // child_count
    source, present = block_source(child_map, parent_count)
    blocks = child_rows.reshape(row_count, child_count, block_size)
    picked = jnp.take(blocks, source, axis=1)
    picked = jnp.where(present[None, :, None], picked, jnp.zeros_like(picked))
    return picked.reshape(row_count, parent_count * block_size)


def parent_rows(child_cols, child_map, parent_count):
    col_count = child_cols.shape[1]
    child_count = child_map.shape[0]
    block_size = child_cols.shape[0] // child_count
    source, present = block_source(child_map, parent_count)
    blocks = child_cols.reshape(child_count, block_size, col_count)
    picked = jnp.take(blocks, source, axis=0)
    picked = jnp.where(present[:, None, None], picked, jnp.zeros_like(picked))
    return picked.reshape(parent_count * block_size, col_count)


def owner_major(parent_cols, inner_count):
    row_count = parent_cols.shape[0]
    sep_part = parent_cols[:, :S].reshape(row_count, inner_count, S // inner_count)
    border_part = parent_cols[:, S:].reshape(row_count, inner_count, B // inner_count)
    return jnp.concatenate([sep_part, border_part], axis=2)


def blocked_cholesky(matrix, panel_size):
    order = matrix.shape[0]
    lower_factor = jnp.zeros_like(matrix)
    trailing = matrix
    inverse_list = []
    for panel_index in range(order // panel_size):
        first = panel_index * panel_size
        last = first + panel_size
        diagonal_block = trailing[first:last, first:last]
        panel_lower = jnp.linalg.cholesky(diagonal_block)
        identity = jnp.eye(panel_size, dtype=jnp.float32)
        inverse = jax.scipy.linalg.solve_triangular(panel_lower, identity, lower=True)
        inverse_list.append(inverse)
        lower_factor = lower_factor.at[first:last, first:last].set(panel_lower)
        if last < order:
            below = jnp.dot(
                trailing[last:, first:last],
                inverse.T,
                precision=HIGHEST,
                preferred_element_type=jnp.float32,
            )
            lower_factor = lower_factor.at[last:, first:last].set(below)
            update = jnp.dot(below, below.T, precision=HIGHEST, preferred_element_type=jnp.float32)
            trailing = trailing.at[last:, last:].add(-update)
    return (lower_factor, inverse_list)


def cholesky_inverse(matrix, base_size):
    order = matrix.shape[0]
    if order <= base_size:
        return base_cholesky_inverse(matrix)
    half = order // 2
    lower_11, inverse_11 = cholesky_inverse(matrix[:half, :half], base_size)
    lower_21 = jnp.dot(matrix[half:, :half], inverse_11.T, precision=HIGH, preferred_element_type=jnp.float32)
    schur = matrix[half:, half:] - jnp.dot(lower_21, lower_21.T, precision=HIGH, preferred_element_type=jnp.float32)
    lower_22, inverse_22 = cholesky_inverse(schur, base_size)
    inverse_21 = -jnp.dot(
        inverse_22,
        jnp.dot(lower_21, inverse_11, precision=HIGH, preferred_element_type=jnp.float32),
        precision=HIGH,
        preferred_element_type=jnp.float32,
    )
    zero = jnp.zeros((half, half), jnp.float32)
    lower = jnp.block([[lower_11, zero], [lower_21, lower_22]])
    inverse = jnp.block([[inverse_11, zero], [inverse_21, inverse_22]])
    return (lower, inverse)


def border_solve(rows_in, lower_factor, inverse_list, panel_size):
    solved = []
    for panel_index in range(len(inverse_list)):
        first = panel_index * panel_size
        pending = rows_in[:, first : first + panel_size]
        for earlier in range(panel_index):
            coupling = lower_factor[
                first : first + panel_size, earlier * panel_size : (earlier + 1) * panel_size
            ]
            pending = pending - jnp.dot(
                solved[earlier], coupling.T, precision=HIGHEST, preferred_element_type=jnp.float32
            )
        solved.append(
            jnp.dot(
                pending,
                inverse_list[panel_index].T,
                precision=HIGHEST,
                preferred_element_type=jnp.float32,
            )
        )
    return jnp.concatenate(solved, axis=1)


def shards(child_update, block_map, obs_design, obs_target):
    inner_count = lax.axis_size("inner")
    group_count = lax.axis_size("outer")
    group_index = lax.axis_index("outer")
    member = lax.axis_index("inner")
    parent_count = (S + B) // BLK
    sep_rows = S // inner_count
    sep_blocks = S // BLK
    panel_size = min(S, 256)
    front_total = sum((group_count >> level_index + 1 for level_index in range(LEVELS)))
    target_total = front_total * sep_blocks
    row_count = obs_design.shape[0]
    step_rows = math.gcd(row_count, 256)
    target_ids = jnp.arange(target_total, dtype=jnp.int32)

    def add_rows(block_index, running):
        design = lax.dynamic_slice_in_dim(obs_design, block_index * step_rows, step_rows, 0)
        labels = lax.dynamic_slice_in_dim(obs_target, block_index * step_rows, step_rows, 0)
        selector = (labels[:, None] == target_ids[None, :]).astype(jnp.bfloat16)
        spread = selector[:, :, None] * design[:, None, :]
        return running + jnp.einsum(
            "rtj,rk->tjk", spread, design, preferred_element_type=jnp.float32
        )

    gram_blocks = lax.fori_loop(
        0, row_count // step_rows, add_rows, jnp.zeros((target_total, BLK, BLK), jnp.float32)
    )
    per_front = gram_blocks.reshape(front_total, S, BLK)
    obs_share = lax.psum_scatter(per_front, "inner", scatter_dimension=1, tiled=True)
    for bit in range(group_count.bit_length() - 1):
        obs_share = obs_share + partner_2(obs_share, "outer", bit)
    current = child_update[0]
    pivot_list = []
    border_list = []
    front_offset = 0
    block_start = member * sep_rows // BLK * BLK
    for level_index in range(LEVELS):
        partner = group_index ^ 1 << level_index
        level_maps = block_map[level_index]
        own_map = lax.dynamic_index_in_dim(level_maps, group_index, 0, keepdims=False)
        sib_map = lax.dynamic_index_in_dim(level_maps, partner, 0, keepdims=False)
        sibling = partner_2(current, "outer", level_index)
        outgoing = jnp.stack(
            [
                owner_major(parent_columns(current, own_map, parent_count), inner_count),
                owner_major(parent_columns(sibling, sib_map, parent_count), inner_count),
            ]
        )
        arrived = lax.all_to_all(outgoing, "inner", split_axis=2, concat_axis=1, tiled=True)
        own_cols = parent_rows(arrived[0, :, 0, :], own_map, parent_count)
        sib_cols = parent_rows(arrived[1, :, 0, :], sib_map, parent_count)
        front_rows = (own_cols + sib_cols).T
        front_slot = front_offset + (group_index >> level_index + 1)
        obs_rows = lax.dynamic_index_in_dim(obs_share, front_slot, 0, keepdims=False)
        sep_front = front_rows[:sep_rows]
        block_now = lax.dynamic_slice_in_dim(sep_front, block_start, BLK, 1)
        sep_front = lax.dynamic_update_slice_in_dim(sep_front, block_now + obs_rows, block_start, 1)
        front_offset = front_offset + (group_count >> level_index + 1)
        pivot_all = lax.all_gather(sep_front[:, :S], "inner", axis=0, tiled=True)
        border_front = front_rows[sep_rows:]
        coupling_all = lax.all_gather(border_front[:, :S], "inner", axis=0, tiled=True)
        half = S // 2
        lower_11, inverse_11 = cholesky_inverse(pivot_all[:half, :half], BLK)
        lower_21 = jnp.dot(
            pivot_all[half:, :half], inverse_11.T, precision=HIGH, preferred_element_type=jnp.float32
        )
        schur = pivot_all[half:, half:] - jnp.dot(
            lower_21, lower_21.T, precision=HIGH, preferred_element_type=jnp.float32
        )
        lower_22, inverse_22 = cholesky_inverse(schur, BLK)
        inverse_21 = -jnp.dot(
            inverse_22,
            jnp.dot(lower_21, inverse_11, precision=HIGH, preferred_element_type=jnp.float32),
            precision=HIGH,
            preferred_element_type=jnp.float32,
        )
        top_count = half // sep_rows
        top_start = jnp.minimum(member, top_count - 1) * sep_rows
        low_start = jnp.maximum(member - top_count, 0) * sep_rows
        top_rows = jnp.concatenate(
            [
                lax.dynamic_slice_in_dim(lower_11, top_start, sep_rows, 0),
                jnp.zeros((sep_rows, half), jnp.float32),
            ],
            axis=1,
        )
        low_rows = jnp.concatenate(
            [
                lax.dynamic_slice_in_dim(lower_21, low_start, sep_rows, 0),
                lax.dynamic_slice_in_dim(lower_22, low_start, sep_rows, 0),
            ],
            axis=1,
        )
        pivot_rows = jnp.where(member < top_count, top_rows, low_rows)
        border_left = jnp.dot(
            coupling_all[:, :half], inverse_11.T, precision=HIGH, preferred_element_type=jnp.float32
        )
        border_right = jnp.dot(
            coupling_all[:, :half], inverse_21.T, precision=HIGH, preferred_element_type=jnp.float32
        ) + jnp.dot(
            coupling_all[:, half:], inverse_22.T, precision=HIGH, preferred_element_type=jnp.float32
        )
        own_rows = B // inner_count
        own_left = lax.dynamic_slice_in_dim(border_left, member * own_rows, own_rows, 0)
        own_right = lax.dynamic_slice_in_dim(border_right, member * own_rows, own_rows, 0)
        border_factor = jnp.concatenate([own_left, own_right], axis=1)
        product = jnp.einsum(
            "rs,cs->rc", own_left, border_left, precision=HIGH, preferred_element_type=jnp.float32
        ) + jnp.einsum(
            "rs,cs->rc", own_right, border_right, precision=HIGH, preferred_element_type=jnp.float32
        )
        current = border_front[:, S:] - product
        pivot_list.append(pivot_rows)
        border_list.append(border_factor)
    pivot_factor = jnp.stack(pivot_list)[:, None]
    border_out = jnp.stack(border_list)[:, None]
    return (pivot_factor, border_out, current[None])


def solution(mesh):
    in_specs = (P("outer", "inner", None), P(), P(("outer", "inner"), None), P(("outer", "inner")))
    out_specs = (
        P(None, "outer", "inner", None),
        P(None, "outer", "inner", None),
        P("outer", "inner", None),
    )
    return jax.shard_map(shards, mesh=mesh, in_specs=in_specs, out_specs=out_specs, check_vma=False)
```
